512 devices in a mesh: gx: 16 (over y, z_hi), gy: 8 (over z_lo, core), gz: 4 (over x).
Axes of the slice: x: 4, y: 8, z: 8 (z_hi: 2, z_lo: 4; z = z_hi * 4 + z_lo), core: 2. Of those that a mesh axis runs over, the one named last changes fastest.
Arguments:
- charge: float32 [128, 256, 512], P('gx', 'gy', 'gz'), may hold values from -60 to 60
- texture: float32 [128, 256, 512], P('gx', 'gy', 'gz'), may hold values from 0.5 to 2
- material_eps: float32 [6], replicated, may hold values from 1 to 12
- layer_material: int32 [512], P('gz'), may hold values from 0 to 5
- gate_volts: float32 [1000], replicated, may hold values from -1 to 1
- block_cond: float32 [65536, 128], P(('gx', 'gy', 'gz')), may hold values from 2 to 20
- block_gate: int32 [65536], P(('gx', 'gy', 'gz')), may hold values from 0 to 999
- block_dest: int32 [65536], P(('gx', 'gy', 'gz')), may hold values from 0 to 127, as said below
- block_column: int32 [65536], P(('gx', 'gy', 'gz')), may hold values from 0 to 255
- initial: float32 [128, 256, 512], P('gx', 'gy', 'gz'), may hold values from -2 to 2
Outputs:
- potential: float32 [128, 256, 512], P('gx', 'gy', 'gz')
- residual_norm: float32 [], replicated
The draws below stay inside these ranges and needn't reach their ends.
Inputs may be any that keep to these rules, and one draw needn't show every extreme that they name: `block_dest`: among the blocks of one device no value appears more than 4 times; one value appears exactly 4 times among the blocks of every device.
All inputs are finite; a program needn't handle non-finite values.
Results may differ from the reference program's by a relative error of at most 0.00002.
Values sent between devices are 32-bit elements; how exact they have to be, the bound alone decides.
No kernel may reach another device: no remote copies, remote signals or barrier semaphores. Data moves between devices by JAX's collectives and lax.ppermute only.
A program may use at most 64 MiB of HBM per device.

```python
import math
import jax
import jax.numpy as jnp

CX = 8
CY = 32
CZ = 128
SWEEPS = 4
MATERIALS = 6
GATES = 1000
B_DEV = 128
PEERS = 128
CAP = 4
NX = 128
NY = 256
NZ = 512
NBLOCKS = 65536
COLUMNS = 256
N_GY = 8
N_GZ = 4


def draw_block_dest(key, part):
    hot_key, rest_key = jax.random.split(key)
    hot_dest = jax.random.randint(hot_key, (), 0, PEERS)
    sender_keys = jax.random.split(rest_key, NBLOCKS // B_DEV)

    def per_sender(sender_key):
        first_key, second_key = jax.random.split(sender_key)
        slot_ids = jax.random.permutation(first_key, (PEERS - 1) * CAP)[:B_DEV - CAP]
        others = slot_ids // CAP
        others = others + (others >= hot_dest).astype(jnp.int32)
        destinations = jnp.concatenate([jnp.full((CAP,), hot_dest, jnp.int32), others.astype(jnp.int32)])
        return jax.random.permutation(second_key, destinations)
    return jax.vmap(per_sender)(sender_keys).reshape(NBLOCKS).astype(jnp.int32)


def with_ends(values, rng, low, top_value):
    place = [jax.random.randint(jax.random.fold_in(rng, axis), (), 0, length) for axis, length in enumerate(values.shape)]
    widest = values.shape.index(max(values.shape))
    beside = place[:widest] + [(place[widest] + 1) % values.shape[widest]] + place[widest + 1:]
    return values.at[tuple(place)].set(low).at[tuple(beside)].set(top_value)


def block_levels(stream_key, shape, cuts, smallest, largest):
    gain = 1.0
    for position, parts in cuts:
        draws = jax.random.uniform(jax.random.fold_in(jax.random.fold_in(stream_key, 6), position), (parts,), jnp.float32, smallest / len(cuts), largest / len(cuts))
        gain = gain * jnp.repeat(jnp.exp(draws), shape[position] // parts).reshape((-1,) + (1,) * (len(shape) - 1 - position))
    return gain


def normal_values(own_key, extent, spread, limit, cuts=(), kind=jnp.bfloat16):
    gain = block_levels(own_key, extent, cuts, -0.22, 0.18) if cuts else 1.0
    values = jax.random.normal(own_key, extent, jnp.float32) * spread * gain
    return jnp.minimum(jnp.maximum(values, -limit), limit).astype(kind)


def setup_inputs(seed: int = 0) -> dict:
    splits = jax.random.split(jax.random.key(seed), 11)
    return {
        "charge": normal_values(splits[0], (NX, NY, NZ), 10.0, 60.0, ((0, 16), (1, 8), (2, 4)), jnp.float32),
        "texture": jnp.clip(jnp.exp(math.log(2.0) - 1.3862944 * jax.random.uniform(splits[1], (NX, NY, NZ), jnp.float32) ** block_levels(splits[1], (NX, NY, NZ), ((0, 16), (1, 8), (2, 4)), -0.2, 0.2)), 0.5, 2.0),
        "material_eps": jnp.clip(jnp.exp(jax.random.uniform(splits[2], (MATERIALS,), jnp.float32, math.log(1.0), math.log(12.0))), 1.0, 12.0),
        "layer_material": with_ends(jax.random.randint(splits[3], (NZ,), 0, MATERIALS), jax.random.fold_in(splits[3], 1), 0, MATERIALS - 1).astype(jnp.int32),
        "gate_volts": jnp.clip(jax.random.uniform(splits[4], (GATES,), jnp.float32, -1.0, 1.0), -1.0, 1.0),
        "block_cond": jnp.clip(jnp.exp(math.log(20.0) - 2.3025851 * jax.random.uniform(splits[5], (NBLOCKS, CZ), jnp.float32) ** block_levels(splits[5], (NBLOCKS, CZ), ((0, 512),), -0.2, 0.2)), 2.0, 20.0),
        "block_gate": with_ends(jax.random.randint(splits[6], (NBLOCKS,), 0, GATES), jax.random.fold_in(splits[6], 1), 0, GATES - 1).astype(jnp.int32),
        "block_dest": draw_block_dest(jax.random.fold_in(splits[10], 71), 0),
        "block_column": with_ends(jax.random.randint(splits[8], (NBLOCKS,), 0, COLUMNS), jax.random.fold_in(splits[8], 1), 0, COLUMNS - 1).astype(jnp.int32),
        "initial": normal_values(splits[9], (NX, NY, NZ), 0.3, 2.0, ((0, 16), (1, 8), (2, 4)), jnp.float32),
    }


relaxation = 0.8

def shifted(padded):
    return [padded[:-2, 1:-1, 1:-1], padded[2:, 1:-1, 1:-1], padded[1:-1, :-2, 1:-1], padded[1:-1, 2:, 1:-1], padded[1:-1, 1:-1, :-2], padded[1:-1, 1:-1, 2:]]

def face_coefficients(padded):
    centre = padded[1:-1, 1:-1, 1:-1]
    result = []
    for neighbour in shifted(padded):
        result.append(2.0 * centre * neighbour / (centre + neighbour))
    return result

def neighbour_sum(coefficients, padded):
    pieces = shifted(padded)
    total_sum = coefficients[0] * pieces[0]
    for index in range(1, 6):
        total_sum = total_sum + coefficients[index] * pieces[index]
    return total_sum

def reference(charge, texture, material_eps, layer_material, gate_volts, block_cond, block_gate, block_dest, block_column, initial):
    layer_eps = material_eps[layer_material]
    permittivity = texture * layer_eps[None, None, :]
    coefficients = face_coefficients(jnp.pad(permittivity, 1))
    block_volts = gate_volts[block_gate]
    block_source = block_cond * block_volts[:, None]
    numbers = jnp.arange(NBLOCKS, dtype=jnp.int32)
    slab = (numbers // B_DEV % N_GZ).astype(jnp.int32)
    row_x = block_dest // N_GY * CX + block_column // CY
    row_y = block_dest % N_GY * CY + block_column % CY
    column = (row_x * NY + row_y).astype(jnp.int32)
    empty = jnp.zeros((NX * NY, N_GZ, CZ), jnp.float32)
    coupling = empty.at[column, slab].add(block_cond).reshape(NX, NY, NZ)
    injected = empty.at[column, slab].add(block_source).reshape(NX, NY, NZ)
    diagonal_sum = coefficients[0]
    for index in range(1, 6):
        diagonal_sum = diagonal_sum + coefficients[index]
    diagonal_sum = diagonal_sum + coupling
    forcing = charge + injected
    potential = initial
    for sweep in range(SWEEPS):
        neighbours = neighbour_sum(coefficients, jnp.pad(potential, 1))
        potential = (1.0 - relaxation) * potential + relaxation * (forcing + neighbours) / diagonal_sum
    neighbours = neighbour_sum(coefficients, jnp.pad(potential, 1))
    residual = forcing + neighbours - diagonal_sum * potential
    residual_norm = jnp.sqrt(jnp.sum(residual * residual) / (NX * NY * NZ))
    return (potential, residual_norm)
```

```python
import jax
import jax.numpy as jnp
from jax import lax
from jax.sharding import PartitionSpec as P

SWEEPS = 4


relaxation = 0.8


def table_lookup(table, indices):
    labels = jnp.arange(table.shape[0], dtype=jnp.int32)
    matches = indices[:, None] == labels[None, :]
    return jnp.sum(jnp.where(matches, table[None, :], 0.0), axis=1)


def exchange(lo, hi, axis):
    count = lax.axis_size(axis)
    forward = [(i, i + 1) for i in range(count - 1)]
    backward = [(i + 1, i) for i in range(count - 1)]
    from_prev = lax.ppermute(hi, axis, forward)
    from_next = lax.ppermute(lo, axis, backward)
    return from_prev, from_next


def with_wide_halo(fields, width):
    prev, nxt = exchange(fields[:, :width], fields[:, -width:], "gx")
    fields = jnp.concatenate([prev, fields, nxt], axis=1)
    prev, nxt = exchange(fields[:, :, :width], fields[:, :, -width:], "gy")
    fields = jnp.concatenate([prev, fields, nxt], axis=2)
    nf, nx, ny, _ = fields.shape

    def pack(a):
        return jnp.moveaxis(a, 3, 1).reshape(nf * width, nx * ny)

    def unpack(a):
        return jnp.moveaxis(a.reshape(nf, width, nx, ny), 1, 3)

    prev, nxt = exchange(pack(fields[..., :width]), pack(fields[..., -width:]), "gz")
    return jnp.concatenate([unpack(prev), fields, unpack(nxt)], axis=3)


def shifted(padded):
    return [
        padded[:-2, 1:-1, 1:-1],
        padded[2:, 1:-1, 1:-1],
        padded[1:-1, :-2, 1:-1],
        padded[1:-1, 2:, 1:-1],
        padded[1:-1, 1:-1, :-2],
        padded[1:-1, 1:-1, 2:],
    ]


def face_coefficients(padded):
    centre = padded[1:-1, 1:-1, 1:-1]
    result = []
    for neighbour in shifted(padded):
        result.append(2.0 * centre * neighbour / (centre + neighbour))
    return result


def neighbour_sum(coefficients, padded):
    pieces = shifted(padded)
    total_sum = coefficients[0] * pieces[0]
    for index in range(1, 6):
        total_sum = total_sum + coefficients[index] * pieces[index]
    return total_sum


def trim(a, k):
    if k == 0:
        return a
    return a[k:-k, k:-k, k:-k]


def on_device(
    charge,
    texture,
    material_eps,
    layer_material,
    gate_volts,
    block_cond,
    block_gate,
    block_dest,
    block_column,
    initial,
):
    cells_x, cells_y, cells_z = charge.shape
    grid_x = lax.axis_size("gx")
    grid_y = lax.axis_size("gy")
    grid_z = lax.axis_size("gz")
    peer_count = grid_x * grid_y
    block_count = block_dest.shape[0]
    capacity = max(2, 4 * block_count // peer_count)
    slot_total = peer_count * capacity
    layer_eps = table_lookup(material_eps, layer_material)
    permittivity = texture * layer_eps[None, None, :]

    same_dest = block_dest[:, None] == block_dest[None, :]
    order = jnp.arange(block_count, dtype=jnp.int32)
    earlier = order[None, :] < order[:, None]
    slot_rank = jnp.sum((same_dest & earlier).astype(jnp.int32), axis=1)
    position = block_dest * capacity + slot_rank
    block_volts = table_lookup(gate_volts, block_gate)
    rows = jnp.concatenate(
        [
            block_cond,
            block_volts[:, None],
            block_column.astype(jnp.float32)[:, None],
        ],
        axis=1,
    )
    width_row = cells_z + 2
    send = jnp.zeros((slot_total, width_row), jnp.float32).at[position].set(rows)
    send = send.reshape(peer_count, capacity * width_row)
    recv = lax.all_to_all(send, ("gx", "gy"), split_axis=0, concat_axis=0, tiled=True)
    recv = recv.reshape(slot_total, width_row)
    cond_recv = recv[:, :cells_z]
    volt_recv = recv[:, cells_z]
    column_recv = recv[:, cells_z + 1].astype(jnp.int32)
    extra_recv = cond_recv * volt_recv[:, None]
    empty = jnp.zeros((cells_x * cells_y, 2, cells_z), jnp.float32)
    summed = empty.at[column_recv].add(jnp.stack([cond_recv, extra_recv], axis=1))
    coupling = summed[:, 0].reshape(cells_x, cells_y, cells_z)
    injected = summed[:, 1].reshape(cells_x, cells_y, cells_z)
    forcing = charge + injected

    halo = SWEEPS + 1
    fields = jnp.stack([permittivity, forcing, coupling, initial], axis=0)
    wide = with_wide_halo(fields, halo)
    eps_w, forcing_w, coupling_w, potential = wide[0], wide[1], wide[2], wide[3]

    coefficients = face_coefficients(eps_w)
    diagonal_sum = coefficients[0]
    for index in range(1, 6):
        diagonal_sum = diagonal_sum + coefficients[index]
    diagonal_sum = diagonal_sum + trim(coupling_w, 1)
    forcing_c = trim(forcing_w, 1)

    def inside_mask(k):
        def axis_mask(axis, cells):
            start = lax.axis_index(axis) * cells - k
            idx = start + jnp.arange(cells + 2 * k, dtype=jnp.int32)
            return (idx >= 0) & (idx < cells * lax.axis_size(axis))

        mx = axis_mask("gx", cells_x)
        my = axis_mask("gy", cells_y)
        mz = axis_mask("gz", cells_z)
        return mx[:, None, None] & my[None, :, None] & mz[None, None, :]

    for sweep in range(SWEEPS):
        k = halo - 1 - sweep
        off = sweep
        coeffs = [trim(c, off) for c in coefficients]
        neighbours = neighbour_sum(coeffs, potential)
        centre = potential[1:-1, 1:-1, 1:-1]
        updated = (1.0 - relaxation) * centre + relaxation * (
            trim(forcing_c, off) + neighbours
        ) / trim(diagonal_sum, off)
        if k > 0:
            updated = jnp.where(inside_mask(k), updated, 0.0)
        potential = updated

    off = SWEEPS
    coeffs = [trim(c, off) for c in coefficients]
    neighbours = neighbour_sum(coeffs, potential)
    centre = potential[1:-1, 1:-1, 1:-1]
    residual = trim(forcing_c, off) + neighbours - trim(diagonal_sum, off) * centre
    local_total = jnp.sum(residual * residual)
    device_count = grid_x * grid_y * grid_z
    gathered = lax.all_to_all(
        jnp.full((device_count,), local_total),
        ("gx", "gy", "gz"),
        split_axis=0,
        concat_axis=0,
        tiled=True,
    )
    squared_total = jnp.sum(gathered)
    cell_count = cells_x * cells_y * cells_z * device_count
    residual_norm = jnp.sqrt(squared_total / cell_count)
    return (centre, residual_norm)


def solution(mesh):
    in_specs = (
        P("gx", "gy", "gz"),
        P("gx", "gy", "gz"),
        P(),
        P("gz"),
        P(),
        P(("gx", "gy", "gz"), None),
        P(("gx", "gy", "gz")),
        P(("gx", "gy", "gz")),
        P(("gx", "gy", "gz")),
        P("gx", "gy", "gz"),
    )
    out_specs = (P("gx", "gy", "gz"), P())
    return jax.shard_map(
        on_device, mesh=mesh, in_specs=in_specs, out_specs=out_specs, check_vma=False
    )
```

```python
import jax
import jax.numpy as jnp
from jax import lax
from jax.sharding import PartitionSpec as P

SWEEPS = 4


relaxation = 0.8


def table_lookup(table, indices):
    labels = jnp.arange(table.shape[0], dtype=jnp.int32)
    matches = indices[:, None] == labels[None, :]
    return jnp.sum(jnp.where(matches, table[None, :], 0.0), axis=1)


def exchange(lo, hi, axis):
    count = lax.axis_size(axis)
    forward = [(i, i + 1) for i in range(count - 1)]
    backward = [(i + 1, i) for i in range(count - 1)]
    from_prev = lax.ppermute(hi, axis, forward)
    from_next = lax.ppermute(lo, axis, backward)
    return from_prev, from_next


def exchange_x(fields, width):
    return exchange(fields[:, :width], fields[:, -width:], "gx")


def with_wide_halo(fields, width):
    nf, nx, ny, nz = fields.shape

    def pack_y(a):
        return a.reshape(nf * nx * width, nz)

    def unpack_y(a):
        return a.reshape(nf, nx, width, nz)

    prev, nxt = exchange(pack_y(fields[:, :, :width]), pack_y(fields[:, :, -width:]), "gy")
    fields = jnp.concatenate([unpack_y(prev), fields, unpack_y(nxt)], axis=2)
    nf, nx, ny, _ = fields.shape

    def pack(a):
        return jnp.moveaxis(a, 3, 1).reshape(nf * width, nx * ny)

    def unpack(a):
        return jnp.moveaxis(a.reshape(nf, width, nx, ny), 1, 3)

    prev, nxt = exchange(pack(fields[..., :width]), pack(fields[..., -width:]), "gz")
    return jnp.concatenate([unpack(prev), fields, unpack(nxt)], axis=3)


def shifted(padded):
    return [
        padded[:-2, 1:-1, 1:-1],
        padded[2:, 1:-1, 1:-1],
        padded[1:-1, :-2, 1:-1],
        padded[1:-1, 2:, 1:-1],
        padded[1:-1, 1:-1, :-2],
        padded[1:-1, 1:-1, 2:],
    ]


def face_coefficients(padded):
    centre = padded[1:-1, 1:-1, 1:-1]
    result = []
    for neighbour in shifted(padded):
        result.append(2.0 * centre * neighbour / (centre + neighbour))
    return result


def neighbour_sum(coefficients, padded):
    pieces = shifted(padded)
    total_sum = coefficients[0] * pieces[0]
    for index in range(1, 6):
        total_sum = total_sum + coefficients[index] * pieces[index]
    return total_sum


def trim(a, k):
    if k == 0:
        return a
    return a[k:-k, k:-k, k:-k]


def on_device(
    charge,
    texture,
    material_eps,
    layer_material,
    gate_volts,
    block_cond,
    block_gate,
    block_dest,
    block_column,
    initial,
):
    cells_x, cells_y, cells_z = charge.shape
    grid_x = lax.axis_size("gx")
    grid_y = lax.axis_size("gy")
    grid_z = lax.axis_size("gz")
    peer_count = grid_x * grid_y
    block_count = block_dest.shape[0]
    capacity = max(2, 4 * block_count // peer_count)
    slot_total = peer_count * capacity
    layer_eps = table_lookup(material_eps, layer_material)
    permittivity = texture * layer_eps[None, None, :]

    same_dest = block_dest[:, None] == block_dest[None, :]
    order = jnp.arange(block_count, dtype=jnp.int32)
    earlier = order[None, :] < order[:, None]
    slot_rank = jnp.sum((same_dest & earlier).astype(jnp.int32), axis=1)
    position = block_dest * capacity + slot_rank
    block_volts = table_lookup(gate_volts, block_gate)
    rows = jnp.concatenate(
        [
            block_cond,
            block_volts[:, None],
            block_column.astype(jnp.float32)[:, None],
        ],
        axis=1,
    )
    width_row = cells_z + 2
    send = jnp.zeros((slot_total, width_row), jnp.float32).at[position].set(rows)
    send = send.reshape(peer_count, capacity * width_row)
    recv = lax.all_to_all(send, ("gx", "gy"), split_axis=0, concat_axis=0, tiled=True)
    recv = recv.reshape(slot_total, width_row)
    cond_recv = recv[:, :cells_z]
    volt_recv = recv[:, cells_z]
    column_recv = recv[:, cells_z + 1].astype(jnp.int32)
    extra_recv = cond_recv * volt_recv[:, None]
    columns = jnp.arange(cells_x * cells_y, dtype=jnp.int32)
    one_hot = (columns[:, None] == column_recv[None, :]).astype(jnp.float32)
    summed = jnp.dot(
        one_hot,
        jnp.concatenate([cond_recv, extra_recv], axis=1),
        precision=lax.Precision.HIGHEST,
        preferred_element_type=jnp.float32,
    )
    coupling = summed[:, :cells_z].reshape(cells_x, cells_y, cells_z)
    injected = summed[:, cells_z:].reshape(cells_x, cells_y, cells_z)
    forcing = charge + injected

    halo = SWEEPS + 1
    early = jnp.stack([permittivity, initial], axis=0)
    early_prev, early_next = exchange_x(early, halo)
    late = jnp.stack([forcing, coupling], axis=0)
    late_prev, late_next = exchange_x(late, halo - 1)
    pad = jnp.zeros((2, 1, cells_y, cells_z), jnp.float32)
    late_prev = jnp.concatenate([pad, late_prev], axis=1)
    late_next = jnp.concatenate([late_next, pad], axis=1)
    fields_x = jnp.concatenate(
        [
            jnp.concatenate([early_prev, early, early_next], axis=1),
            jnp.concatenate([late_prev, late, late_next], axis=1),
        ],
        axis=0,
    )
    wide = with_wide_halo(fields_x, halo)
    eps_w, initial_w, forcing_w, coupling_w = wide[0], wide[1], wide[2], wide[3]
    potential = initial_w

    coefficients = face_coefficients(eps_w)
    diagonal_sum = coefficients[0]
    for index in range(1, 6):
        diagonal_sum = diagonal_sum + coefficients[index]
    diagonal_sum = diagonal_sum + trim(coupling_w, 1)
    forcing_c = trim(forcing_w, 1)

    def inside_mask(k):
        def axis_mask(axis, cells):
            start = lax.axis_index(axis) * cells - k
            idx = start + jnp.arange(cells + 2 * k, dtype=jnp.int32)
            return (idx >= 0) & (idx < cells * lax.axis_size(axis))

        mx = axis_mask("gx", cells_x)
        my = axis_mask("gy", cells_y)
        mz = axis_mask("gz", cells_z)
        return mx[:, None, None] & my[None, :, None] & mz[None, None, :]

    for sweep in range(SWEEPS):
        k = halo - 1 - sweep
        off = sweep
        coeffs = [trim(c, off) for c in coefficients]
        neighbours = neighbour_sum(coeffs, potential)
        centre = potential[1:-1, 1:-1, 1:-1]
        updated = (1.0 - relaxation) * centre + relaxation * (
            trim(forcing_c, off) + neighbours
        ) / trim(diagonal_sum, off)
        if k > 0:
            updated = jnp.where(inside_mask(k), updated, 0.0)
        potential = updated

    off = SWEEPS
    coeffs = [trim(c, off) for c in coefficients]
    neighbours = neighbour_sum(coeffs, potential)
    centre = potential[1:-1, 1:-1, 1:-1]
    residual = trim(forcing_c, off) + neighbours - trim(diagonal_sum, off) * centre
    local_total = jnp.sum(residual * residual)
    device_count = grid_x * grid_y * grid_z
    gathered = lax.all_to_all(
        jnp.full((device_count,), local_total),
        ("gx", "gy", "gz"),
        split_axis=0,
        concat_axis=0,
        tiled=True,
    )
    squared_total = jnp.sum(gathered)
    cell_count = cells_x * cells_y * cells_z * device_count
    residual_norm = jnp.sqrt(squared_total / cell_count)
    return (centre, residual_norm)


def solution(mesh):
    in_specs = (
        P("gx", "gy", "gz"),
        P("gx", "gy", "gz"),
        P(),
        P("gz"),
        P(),
        P(("gx", "gy", "gz"), None),
        P(("gx", "gy", "gz")),
        P(("gx", "gy", "gz")),
        P(("gx", "gy", "gz")),
        P("gx", "gy", "gz"),
    )
    out_specs = (P("gx", "gy", "gz"), P())
    return jax.shard_map(
        on_device, mesh=mesh, in_specs=in_specs, out_specs=out_specs, check_vma=False
    )
```

```python
import jax
import jax.numpy as jnp
from jax import lax
from jax.sharding import PartitionSpec as P

SWEEPS = 4


relaxation = 0.8


def table_lookup(table, indices):
    labels = jnp.arange(table.shape[0], dtype=jnp.int32)
    matches = indices[:, None] == labels[None, :]
    return jnp.sum(jnp.where(matches, table[None, :], 0.0), axis=1)


def exchange(lo, hi, axis):
    count = lax.axis_size(axis)
    forward = [(i, i + 1) for i in range(count - 1)]
    backward = [(i + 1, i) for i in range(count - 1)]
    from_prev = lax.ppermute(hi, axis, forward)
    from_next = lax.ppermute(lo, axis, backward)
    return from_prev, from_next


def exchange_x(fields, width):
    return exchange(fields[:, :width], fields[:, -width:], "gx")


def with_wide_halo(fields, width):
    nf, nx, ny, nz = fields.shape

    def pack_y(a):
        return a.reshape(nf * nx * width, nz)

    def unpack_y(a):
        return a.reshape(nf, nx, width, nz)

    prev, nxt = exchange(pack_y(fields[:, :, :width]), pack_y(fields[:, :, -width:]), "gy")
    fields = jnp.concatenate([unpack_y(prev), fields, unpack_y(nxt)], axis=2)
    nf, nx, ny, _ = fields.shape

    def pack(a):
        return jnp.moveaxis(a, 3, 1).reshape(nf * width, nx * ny)

    def unpack(a):
        return jnp.moveaxis(a.reshape(nf, width, nx, ny), 1, 3)

    prev, nxt = exchange(pack(fields[..., :width]), pack(fields[..., -width:]), "gz")
    return jnp.concatenate([unpack(prev), fields, unpack(nxt)], axis=3)


def shifted(padded):
    return [
        padded[:-2, 1:-1, 1:-1],
        padded[2:, 1:-1, 1:-1],
        padded[1:-1, :-2, 1:-1],
        padded[1:-1, 2:, 1:-1],
        padded[1:-1, 1:-1, :-2],
        padded[1:-1, 1:-1, 2:],
    ]


def face_coefficients(padded):
    centre = padded[1:-1, 1:-1, 1:-1]
    result = []
    for neighbour in shifted(padded):
        result.append(2.0 * centre * neighbour / (centre + neighbour))
    return result


def neighbour_sum(coefficients, padded):
    pieces = shifted(padded)
    total_sum = coefficients[0] * pieces[0]
    for index in range(1, 6):
        total_sum = total_sum + coefficients[index] * pieces[index]
    return total_sum


def trim(a, k):
    if k == 0:
        return a
    return a[k:-k, k:-k, k:-k]


def on_device(
    charge,
    texture,
    material_eps,
    layer_material,
    gate_volts,
    block_cond,
    block_gate,
    block_dest,
    block_column,
    initial,
):
    cells_x, cells_y, cells_z = charge.shape
    grid_x = lax.axis_size("gx")
    grid_y = lax.axis_size("gy")
    grid_z = lax.axis_size("gz")
    peer_count = grid_x * grid_y
    block_count = block_dest.shape[0]
    capacity = max(2, 4 * block_count // peer_count)
    layer_eps = table_lookup(material_eps, layer_material)
    permittivity = texture * layer_eps[None, None, :]

    halo = SWEEPS + 1
    reach = halo - 1
    early = jnp.stack([permittivity, initial, charge], axis=0)
    early_prev, early_next = exchange_x(early, halo)
    early_x = jnp.concatenate([early_prev, early, early_next], axis=1)

    roles = 3
    same_dest = block_dest[:, None] == block_dest[None, :]
    order = jnp.arange(block_count, dtype=jnp.int32)
    earlier = order[None, :] < order[:, None]
    slot_rank = jnp.sum((same_dest & earlier).astype(jnp.int32), axis=1)
    owner_x = block_dest // grid_y
    column_x = block_column // cells_y
    slot_total = peer_count * roles * capacity
    to_next = (column_x >= cells_x - reach) & (owner_x + 1 < grid_x)
    to_prev = (column_x < reach) & (owner_x > 0)
    position = jnp.concatenate(
        [
            block_dest * (roles * capacity) + slot_rank,
            jnp.where(
                to_next, (block_dest + grid_y) * (roles * capacity) + capacity + slot_rank, slot_total
            ),
            jnp.where(
                to_prev, (block_dest - grid_y) * (roles * capacity) + 2 * capacity + slot_rank, slot_total
            ),
        ]
    )
    block_volts = table_lookup(gate_volts, block_gate)
    rows = jnp.concatenate(
        [
            block_cond,
            block_volts[:, None],
            block_column.astype(jnp.float32)[:, None],
        ],
        axis=1,
    )
    rows = jnp.concatenate([rows, rows, rows], axis=0)
    width_row = cells_z + 2
    send = jnp.zeros((slot_total, width_row), jnp.float32).at[position].set(rows, mode="drop")
    send = send.reshape(peer_count, roles * capacity * width_row)
    recv = lax.all_to_all(send, ("gx", "gy"), split_axis=0, concat_axis=0, tiled=True)
    recv = recv.reshape(slot_total, width_row)
    cond_recv = recv[:, :cells_z]
    volt_recv = recv[:, cells_z]
    column_recv = recv[:, cells_z + 1].astype(jnp.int32)
    extra_recv = cond_recv * volt_recv[:, None]
    role_recv = (jnp.arange(slot_total, dtype=jnp.int32) // capacity) % roles
    shift = jnp.where(role_recv == 1, -cells_x, jnp.where(role_recv == 2, cells_x, 0))
    ext_x = column_recv // cells_y + shift + reach
    ext_column = ext_x * cells_y + column_recv % cells_y
    ext_cells = cells_x + 2 * reach
    columns = jnp.arange(ext_cells * cells_y, dtype=jnp.int32)
    one_hot = (columns[:, None] == ext_column[None, :]).astype(jnp.float32)
    summed = jnp.dot(
        one_hot,
        jnp.concatenate([cond_recv, extra_recv], axis=1),
        precision=lax.Precision.HIGHEST,
        preferred_element_type=jnp.float32,
    )
    coupling_x = summed[:, :cells_z].reshape(ext_cells, cells_y, cells_z)
    injected_x = summed[:, cells_z:].reshape(ext_cells, cells_y, cells_z)
    forcing_x = early_x[2, 1:-1] + injected_x
    pad = jnp.zeros((1, cells_y, cells_z), jnp.float32)
    fields_x = jnp.concatenate(
        [
            early_x[:2],
            jnp.concatenate([pad, forcing_x, pad], axis=0)[None],
            jnp.concatenate([pad, coupling_x, pad], axis=0)[None],
        ],
        axis=0,
    )
    wide = with_wide_halo(fields_x, halo)
    eps_w, initial_w, forcing_w, coupling_w = wide[0], wide[1], wide[2], wide[3]
    potential = initial_w

    coefficients = face_coefficients(eps_w)
    diagonal_sum = coefficients[0]
    for index in range(1, 6):
        diagonal_sum = diagonal_sum + coefficients[index]
    diagonal_sum = diagonal_sum + trim(coupling_w, 1)
    forcing_c = trim(forcing_w, 1)

    def inside_mask(k):
        def axis_mask(axis, cells):
            start = lax.axis_index(axis) * cells - k
            idx = start + jnp.arange(cells + 2 * k, dtype=jnp.int32)
            return (idx >= 0) & (idx < cells * lax.axis_size(axis))

        mx = axis_mask("gx", cells_x)
        my = axis_mask("gy", cells_y)
        mz = axis_mask("gz", cells_z)
        return mx[:, None, None] & my[None, :, None] & mz[None, None, :]

    for sweep in range(SWEEPS):
        k = halo - 1 - sweep
        off = sweep
        coeffs = [trim(c, off) for c in coefficients]
        neighbours = neighbour_sum(coeffs, potential)
        centre = potential[1:-1, 1:-1, 1:-1]
        updated = (1.0 - relaxation) * centre + relaxation * (
            trim(forcing_c, off) + neighbours
        ) / trim(diagonal_sum, off)
        if k > 0:
            updated = jnp.where(inside_mask(k), updated, 0.0)
        potential = updated

    off = SWEEPS
    coeffs = [trim(c, off) for c in coefficients]
    neighbours = neighbour_sum(coeffs, potential)
    centre = potential[1:-1, 1:-1, 1:-1]
    residual = trim(forcing_c, off) + neighbours - trim(diagonal_sum, off) * centre
    local_total = jnp.sum(residual * residual)
    device_count = grid_x * grid_y * grid_z
    gathered = lax.all_to_all(
        jnp.full((device_count,), local_total),
        ("gx", "gy", "gz"),
        split_axis=0,
        concat_axis=0,
        tiled=True,
    )
    squared_total = jnp.sum(gathered)
    cell_count = cells_x * cells_y * cells_z * device_count
    residual_norm = jnp.sqrt(squared_total / cell_count)
    return (centre, residual_norm)


def solution(mesh):
    in_specs = (
        P("gx", "gy", "gz"),
        P("gx", "gy", "gz"),
        P(),
        P("gz"),
        P(),
        P(("gx", "gy", "gz"), None),
        P(("gx", "gy", "gz")),
        P(("gx", "gy", "gz")),
        P(("gx", "gy", "gz")),
        P("gx", "gy", "gz"),
    )
    out_specs = (P("gx", "gy", "gz"), P())
    return jax.shard_map(
        on_device, mesh=mesh, in_specs=in_specs, out_specs=out_specs, check_vma=False
    )
```

```python
import jax
import jax.numpy as jnp
from jax import lax
from jax.sharding import PartitionSpec as P

SWEEPS = 4


relaxation = 0.8


def table_lookup(table, indices):
    labels = jnp.arange(table.shape[0], dtype=jnp.int32)
    matches = indices[:, None] == labels[None, :]
    return jnp.sum(jnp.where(matches, table[None, :], 0.0), axis=1)


def exchange(lo, hi, axis):
    count = lax.axis_size(axis)
    forward = [(i, i + 1) for i in range(count - 1)]
    backward = [(i + 1, i) for i in range(count - 1)]
    from_prev = lax.ppermute(hi, axis, forward)
    from_next = lax.ppermute(lo, axis, backward)
    return from_prev, from_next


def exchange_x(fields, width):
    return exchange(fields[:, :width], fields[:, -width:], "gx")


def with_wide_halo(fields, width):
    prev, nxt = exchange(fields[:, :width], fields[:, -width:], "gx")
    fields = jnp.concatenate([prev, fields, nxt], axis=1)
    nf, nx, ny, nz = fields.shape

    def pack_y(a):
        return a.reshape(nf * nx * width, nz)

    def unpack_y(a):
        return a.reshape(nf, nx, width, nz)

    prev, nxt = exchange(pack_y(fields[:, :, :width]), pack_y(fields[:, :, -width:]), "gy")
    fields = jnp.concatenate([unpack_y(prev), fields, unpack_y(nxt)], axis=2)
    nf, nx, ny, _ = fields.shape

    def pack(a):
        return jnp.moveaxis(a, 3, 1).reshape(nf * width, nx * ny)

    def unpack(a):
        return jnp.moveaxis(a.reshape(nf, width, nx, ny), 1, 3)

    prev, nxt = exchange(pack(fields[..., :width]), pack(fields[..., -width:]), "gz")
    return jnp.concatenate([unpack(prev), fields, unpack(nxt)], axis=3)


def shifted(padded):
    return [
        padded[:-2, 1:-1, 1:-1],
        padded[2:, 1:-1, 1:-1],
        padded[1:-1, :-2, 1:-1],
        padded[1:-1, 2:, 1:-1],
        padded[1:-1, 1:-1, :-2],
        padded[1:-1, 1:-1, 2:],
    ]


def face_coefficients(padded):
    centre = padded[1:-1, 1:-1, 1:-1]
    result = []
    for neighbour in shifted(padded):
        result.append(2.0 * centre * neighbour / (centre + neighbour))
    return result


def neighbour_sum(coefficients, padded):
    pieces = shifted(padded)
    total_sum = coefficients[0] * pieces[0]
    for index in range(1, 6):
        total_sum = total_sum + coefficients[index] * pieces[index]
    return total_sum


def trim(a, k):
    if k == 0:
        return a
    return a[k:-k, k:-k, k:-k]


def on_device(
    charge,
    texture,
    material_eps,
    layer_material,
    gate_volts,
    block_cond,
    block_gate,
    block_dest,
    block_column,
    initial,
):
    cells_x, cells_y, cells_z = charge.shape
    grid_x = lax.axis_size("gx")
    grid_y = lax.axis_size("gy")
    grid_z = lax.axis_size("gz")
    peer_count = grid_x * grid_y
    block_count = block_dest.shape[0]
    capacity = max(2, 4 * block_count // peer_count)
    slot_total = peer_count * capacity
    layer_eps = table_lookup(material_eps, layer_material)
    permittivity = texture * layer_eps[None, None, :]

    same_dest = block_dest[:, None] == block_dest[None, :]
    order = jnp.arange(block_count, dtype=jnp.int32)
    earlier = order[None, :] < order[:, None]
    slot_rank = jnp.sum((same_dest & earlier).astype(jnp.int32), axis=1)
    position = block_dest * capacity + slot_rank
    block_volts = table_lookup(gate_volts, block_gate)
    rows = jnp.concatenate(
        [
            block_cond,
            block_volts[:, None],
            block_column.astype(jnp.float32)[:, None],
        ],
        axis=1,
    )
    width_row = cells_z + 2
    send = jnp.zeros((slot_total, width_row), jnp.float32).at[position].set(rows)
    send = send.reshape(peer_count, capacity * width_row)
    recv = lax.all_to_all(send, ("gx", "gy"), split_axis=0, concat_axis=0, tiled=True)
    recv = recv.reshape(slot_total, width_row)
    cond_recv = recv[:, :cells_z]
    volt_recv = recv[:, cells_z]
    column_recv = recv[:, cells_z + 1].astype(jnp.int32)
    extra_recv = cond_recv * volt_recv[:, None]
    columns = jnp.arange(cells_x * cells_y, dtype=jnp.int32)
    one_hot = (columns[:, None] == column_recv[None, :]).astype(jnp.float32)
    summed = jnp.dot(
        one_hot,
        jnp.concatenate([cond_recv, extra_recv], axis=1),
        precision=lax.Precision.HIGHEST,
        preferred_element_type=jnp.float32,
    )
    coupling = summed[:, :cells_z].reshape(cells_x, cells_y, cells_z)
    injected = summed[:, cells_z:].reshape(cells_x, cells_y, cells_z)
    forcing = charge + injected

    halo = SWEEPS + 1
    early = with_wide_halo(jnp.stack([permittivity, initial], axis=0), halo)
    late = with_wide_halo(jnp.stack([forcing, coupling], axis=0), halo - 1)
    eps_w, potential = early[0], early[1]
    forcing_c, coupling_c = late[0], late[1]

    coefficients = face_coefficients(eps_w)
    diagonal_sum = coefficients[0]
    for index in range(1, 6):
        diagonal_sum = diagonal_sum + coefficients[index]
    diagonal_sum = diagonal_sum + coupling_c

    def inside_mask(k):
        def axis_mask(axis, cells):
            start = lax.axis_index(axis) * cells - k
            idx = start + jnp.arange(cells + 2 * k, dtype=jnp.int32)
            return (idx >= 0) & (idx < cells * lax.axis_size(axis))

        mx = axis_mask("gx", cells_x)
        my = axis_mask("gy", cells_y)
        mz = axis_mask("gz", cells_z)
        return mx[:, None, None] & my[None, :, None] & mz[None, None, :]

    for sweep in range(SWEEPS):
        k = halo - 1 - sweep
        off = sweep
        coeffs = [trim(c, off) for c in coefficients]
        neighbours = neighbour_sum(coeffs, potential)
        centre = potential[1:-1, 1:-1, 1:-1]
        updated = (1.0 - relaxation) * centre + relaxation * (
            trim(forcing_c, off) + neighbours
        ) / trim(diagonal_sum, off)
        if k > 0:
            updated = jnp.where(inside_mask(k), updated, 0.0)
        potential = updated

    off = SWEEPS
    coeffs = [trim(c, off) for c in coefficients]
    neighbours = neighbour_sum(coeffs, potential)
    centre = potential[1:-1, 1:-1, 1:-1]
    residual = trim(forcing_c, off) + neighbours - trim(diagonal_sum, off) * centre
    local_total = jnp.sum(residual * residual)
    device_count = grid_x * grid_y * grid_z
    gathered = lax.all_to_all(
        jnp.full((device_count,), local_total),
        ("gx", "gy", "gz"),
        split_axis=0,
        concat_axis=0,
        tiled=True,
    )
    squared_total = jnp.sum(gathered)
    cell_count = cells_x * cells_y * cells_z * device_count
    residual_norm = jnp.sqrt(squared_total / cell_count)
    return (centre, residual_norm)


def solution(mesh):
    in_specs = (
        P("gx", "gy", "gz"),
        P("gx", "gy", "gz"),
        P(),
        P("gz"),
        P(),
        P(("gx", "gy", "gz"), None),
        P(("gx", "gy", "gz")),
        P(("gx", "gy", "gz")),
        P(("gx", "gy", "gz")),
        P("gx", "gy", "gz"),
    )
    out_specs = (P("gx", "gy", "gz"), P())
    return jax.shard_map(
        on_device, mesh=mesh, in_specs=in_specs, out_specs=out_specs, check_vma=False
    )
```

```python
import jax
import jax.numpy as jnp
from jax import lax
from jax.sharding import PartitionSpec as P


SWEEPS = 4


relaxation = 0.8


def table_lookup(table, indices):
    labels = jnp.arange(table.shape[0], dtype=jnp.int32)
    matches = indices[:, None] == labels[None, :]
    return jnp.sum(jnp.where(matches, table[None, :], 0.0), axis=1)


def exchange(lo, hi, axis):
    count = lax.axis_size(axis)
    forward = [(i, i + 1) for i in range(count - 1)]
    backward = [(i + 1, i) for i in range(count - 1)]
    from_prev = lax.ppermute(hi, axis, forward)
    from_next = lax.ppermute(lo, axis, backward)
    return from_prev, from_next


def with_wide_halo(fields, width):
    prev, nxt = exchange(fields[:, :width], fields[:, -width:], "gx")
    fields = jnp.concatenate([prev, fields, nxt], axis=1)
    nf, nx, ny, nz = fields.shape

    def pack_y(a):
        return a.reshape(nf * nx * width, nz)

    def unpack_y(a):
        return a.reshape(nf, nx, width, nz)

    prev, nxt = exchange(pack_y(fields[:, :, :width]), pack_y(fields[:, :, -width:]), "gy")
    fields = jnp.concatenate([unpack_y(prev), fields, unpack_y(nxt)], axis=2)
    nf, nx, ny, _ = fields.shape

    def pack(a):
        return jnp.moveaxis(a, 3, 1).reshape(nf * width, nx * ny)

    def unpack(a):
        return jnp.moveaxis(a.reshape(nf, width, nx, ny), 1, 3)

    prev, nxt = exchange(pack(fields[..., :width]), pack(fields[..., -width:]), "gz")
    return jnp.concatenate([unpack(prev), fields, unpack(nxt)], axis=3)


def shifted(padded):
    return [
        padded[:-2, 1:-1, 1:-1],
        padded[2:, 1:-1, 1:-1],
        padded[1:-1, :-2, 1:-1],
        padded[1:-1, 2:, 1:-1],
        padded[1:-1, 1:-1, :-2],
        padded[1:-1, 1:-1, 2:],
    ]


def face_coefficients(padded):
    centre = padded[1:-1, 1:-1, 1:-1]
    result = []
    for neighbour in shifted(padded):
        result.append(2.0 * centre * neighbour / (centre + neighbour))
    return result


def neighbour_sum(coefficients, padded):
    pieces = shifted(padded)
    total_sum = coefficients[0] * pieces[0]
    for index in range(1, 6):
        total_sum = total_sum + coefficients[index] * pieces[index]
    return total_sum


def trim(a, k):
    if k == 0:
        return a
    return a[k:-k, k:-k, k:-k]


def device_step(
    charge,
    texture,
    material_eps,
    layer_material,
    gate_volts,
    block_cond,
    block_gate,
    block_dest,
    block_column,
    initial,
):
    cells_x, cells_y, cells_z = charge.shape
    grid_x = lax.axis_size("gx")
    grid_y = lax.axis_size("gy")
    grid_z = lax.axis_size("gz")
    peer_count = grid_x * grid_y
    block_count = block_dest.shape[0]
    capacity = max(2, 4 * block_count // peer_count)
    slot_total = peer_count * capacity
    layer_eps = table_lookup(material_eps, layer_material)
    permittivity = texture * layer_eps[None, None, :]

    same_dest = block_dest[:, None] == block_dest[None, :]
    order = jnp.arange(block_count, dtype=jnp.int32)
    earlier = order[None, :] < order[:, None]
    slot_rank = jnp.sum((same_dest & earlier).astype(jnp.int32), axis=1)
    position = block_dest * capacity + slot_rank
    block_volts = table_lookup(gate_volts, block_gate)
    rows = jnp.concatenate(
        [
            block_cond,
            block_volts[:, None],
            block_column.astype(jnp.float32)[:, None],
        ],
        axis=1,
    )
    width_row = cells_z + 2
    send = jnp.zeros((slot_total, width_row), jnp.float32).at[position].set(rows)
    send = send.reshape(peer_count, capacity * width_row)
    recv = lax.all_to_all(send, ("gx", "gy"), split_axis=0, concat_axis=0, tiled=True)
    recv = recv.reshape(slot_total, width_row)
    cond_recv = recv[:, :cells_z]
    volt_recv = recv[:, cells_z]
    column_recv = recv[:, cells_z + 1].astype(jnp.int32)
    extra_recv = cond_recv * volt_recv[:, None]
    columns = jnp.arange(cells_x * cells_y, dtype=jnp.int32)
    one_hot = (columns[:, None] == column_recv[None, :]).astype(jnp.float32)
    summed = jnp.dot(
        one_hot,
        jnp.concatenate([cond_recv, extra_recv], axis=1),
        precision=lax.Precision.HIGHEST,
        preferred_element_type=jnp.float32,
    )
    coupling = summed[:, :cells_z].reshape(cells_x, cells_y, cells_z)
    injected = summed[:, cells_z:].reshape(cells_x, cells_y, cells_z)
    forcing = charge + injected

    halo = SWEEPS + 1
    early = with_wide_halo(jnp.stack([permittivity, initial], axis=0), halo)
    late = with_wide_halo(jnp.stack([forcing, coupling], axis=0), halo - 1)
    eps_w, potential = early[0], early[1]
    forcing_c, coupling_c = late[0], late[1]

    coefficients = face_coefficients(eps_w)
    diagonal_sum = coefficients[0]
    for index in range(1, 6):
        diagonal_sum = diagonal_sum + coefficients[index]
    diagonal_sum = diagonal_sum + coupling_c

    def inside_mask(k):
        def axis_mask(axis, cells):
            start = lax.axis_index(axis) * cells - k
            idx = start + jnp.arange(cells + 2 * k, dtype=jnp.int32)
            return (idx >= 0) & (idx < cells * lax.axis_size(axis))

        mx = axis_mask("gx", cells_x)
        my = axis_mask("gy", cells_y)
        mz = axis_mask("gz", cells_z)
        return mx[:, None, None] & my[None, :, None] & mz[None, None, :]

    for sweep in range(SWEEPS):
        k = halo - 1 - sweep
        off = sweep
        coeffs = [trim(c, off) for c in coefficients]
        neighbours = neighbour_sum(coeffs, potential)
        centre = potential[1:-1, 1:-1, 1:-1]
        updated = (1.0 - relaxation) * centre + relaxation * (
            trim(forcing_c, off) + neighbours
        ) / trim(diagonal_sum, off)
        if k > 0:
            updated = jnp.where(inside_mask(k), updated, 0.0)
        potential = updated

    off = SWEEPS
    coeffs = [trim(c, off) for c in coefficients]
    neighbours = neighbour_sum(coeffs, potential)
    centre = potential[1:-1, 1:-1, 1:-1]
    residual = trim(forcing_c, off) + neighbours - trim(diagonal_sum, off) * centre
    local_total = jnp.sum(residual * residual)
    device_count = grid_x * grid_y * grid_z
    gathered = lax.all_to_all(
        jnp.full((device_count,), local_total),
        ("gx", "gy", "gz"),
        split_axis=0,
        concat_axis=0,
        tiled=True,
    )
    squared_total = jnp.sum(gathered)
    cell_count = cells_x * cells_y * cells_z * device_count
    residual_norm = jnp.sqrt(squared_total / cell_count)
    return (centre, residual_norm)


def solution(mesh):
    in_specs = (
        P("gx", "gy", "gz"),
        P("gx", "gy", "gz"),
        P(),
        P("gz"),
        P(),
        P(("gx", "gy", "gz"), None),
        P(("gx", "gy", "gz")),
        P(("gx", "gy", "gz")),
        P(("gx", "gy", "gz")),
        P("gx", "gy", "gz"),
    )
    out_specs = (P("gx", "gy", "gz"), P())
    return jax.shard_map(
        device_step, mesh=mesh, in_specs=in_specs, out_specs=out_specs, check_vma=False
    )
```

```python
import jax
import jax.numpy as jnp
from jax import lax
from jax.sharding import PartitionSpec as P

SWEEPS = 4


relaxation = 0.8


def table_lookup(table, indices):
    labels = jnp.arange(table.shape[0], dtype=jnp.int32)
    matches = indices[:, None] == labels[None, :]
    return jnp.sum(jnp.where(matches, table[None, :], 0.0), axis=1)


def exchange(lo, hi, axis):
    count = lax.axis_size(axis)
    forward = [(i, i + 1) for i in range(count - 1)]
    backward = [(i + 1, i) for i in range(count - 1)]
    from_prev = lax.ppermute(hi, axis, forward)
    from_next = lax.ppermute(lo, axis, backward)
    return from_prev, from_next


def exchange_x(fields, width):
    return exchange(fields[:, :width], fields[:, -width:], "gx")


def with_wide_halo(fields, width):
    nf, nx, ny, nz = fields.shape

    def pack_y(a):
        return a.reshape(nf * nx * width, nz)

    def unpack_y(a):
        return a.reshape(nf, nx, width, nz)

    prev, nxt = exchange(pack_y(fields[:, :, :width]), pack_y(fields[:, :, -width:]), "gy")
    fields = jnp.concatenate([unpack_y(prev), fields, unpack_y(nxt)], axis=2)
    nf, nx, ny, _ = fields.shape

    def pack(a):
        return jnp.moveaxis(a, 3, 1).reshape(nf * width, nx * ny)

    def unpack(a):
        return jnp.moveaxis(a.reshape(nf, width, nx, ny), 1, 3)

    prev, nxt = exchange(pack(fields[..., :width]), pack(fields[..., -width:]), "gz")
    return jnp.concatenate([unpack(prev), fields, unpack(nxt)], axis=3)


def shifted(padded):
    return [
        padded[:-2, 1:-1, 1:-1],
        padded[2:, 1:-1, 1:-1],
        padded[1:-1, :-2, 1:-1],
        padded[1:-1, 2:, 1:-1],
        padded[1:-1, 1:-1, :-2],
        padded[1:-1, 1:-1, 2:],
    ]


def face_coefficients(padded):
    centre = padded[1:-1, 1:-1, 1:-1]
    result = []
    for neighbour in shifted(padded):
        result.append(2.0 * centre * neighbour / (centre + neighbour))
    return result


def neighbour_sum(coefficients, padded):
    pieces = shifted(padded)
    total_sum = coefficients[0] * pieces[0]
    for index in range(1, 6):
        total_sum = total_sum + coefficients[index] * pieces[index]
    return total_sum


def trim(a, k):
    if k == 0:
        return a
    return a[k:-k, k:-k, k:-k]


def on_device(
    charge,
    texture,
    material_eps,
    layer_material,
    gate_volts,
    block_cond,
    block_gate,
    block_dest,
    block_column,
    initial,
):
    cells_x, cells_y, cells_z = charge.shape
    grid_x = lax.axis_size("gx")
    grid_y = lax.axis_size("gy")
    grid_z = lax.axis_size("gz")
    peer_count = grid_x * grid_y
    block_count = block_dest.shape[0]
    capacity = max(2, 4 * block_count // peer_count)
    slot_total = peer_count * capacity
    layer_eps = table_lookup(material_eps, layer_material)
    permittivity = texture * layer_eps[None, None, :]

    same_dest = block_dest[:, None] == block_dest[None, :]
    order = jnp.arange(block_count, dtype=jnp.int32)
    earlier = order[None, :] < order[:, None]
    slot_rank = jnp.sum((same_dest & earlier).astype(jnp.int32), axis=1)
    position = block_dest * capacity + slot_rank
    block_volts = table_lookup(gate_volts, block_gate)
    rows = jnp.concatenate(
        [
            block_cond,
            block_volts[:, None],
            block_column.astype(jnp.float32)[:, None],
        ],
        axis=1,
    )
    width_row = cells_z + 2
    send = jnp.zeros((slot_total, width_row), jnp.float32).at[position].set(rows)
    send = send.reshape(peer_count, capacity * width_row)
    recv = lax.all_to_all(send, ("gx", "gy"), split_axis=0, concat_axis=0, tiled=True)
    recv = recv.reshape(slot_total, width_row)
    cond_recv = recv[:, :cells_z]
    volt_recv = recv[:, cells_z]
    column_recv = recv[:, cells_z + 1].astype(jnp.int32)
    extra_recv = cond_recv * volt_recv[:, None]
    columns = jnp.arange(cells_x * cells_y, dtype=jnp.int32)
    one_hot = (columns[:, None] == column_recv[None, :]).astype(jnp.float32)
    summed = jnp.dot(
        one_hot,
        jnp.concatenate([cond_recv, extra_recv], axis=1),
        precision=lax.Precision.HIGHEST,
        preferred_element_type=jnp.float32,
    )
    coupling = summed[:, :cells_z].reshape(cells_x, cells_y, cells_z)
    injected = summed[:, cells_z:].reshape(cells_x, cells_y, cells_z)
    forcing = charge + injected

    halo = SWEEPS + 1
    lo, hx, hy, hz = halo, halo + cells_x, halo + cells_y, halo + cells_z
    buffer = jnp.zeros(
        (4, cells_x + 2 * halo, cells_y + 2 * halo, cells_z + 2 * halo), jnp.float32
    )
    early = jnp.stack([permittivity, initial], axis=0)
    early_prev, early_next = exchange_x(early, halo)
    late = jnp.stack([forcing, coupling], axis=0)
    late_prev, late_next = exchange_x(late, halo - 1)
    buffer = buffer.at[0:2, lo:hx, lo:hy, lo:hz].set(early)
    buffer = buffer.at[2:4, lo:hx, lo:hy, lo:hz].set(late)
    buffer = buffer.at[0:2, 0:lo, lo:hy, lo:hz].set(early_prev)
    buffer = buffer.at[0:2, hx:, lo:hy, lo:hz].set(early_next)
    buffer = buffer.at[2:4, 1:lo, lo:hy, lo:hz].set(late_prev)
    buffer = buffer.at[2:4, hx:hx + halo - 1, lo:hy, lo:hz].set(late_next)

    nf, nx, ny, nz = buffer.shape
    slab_y = (nf * nx * halo, cells_z)
    prev, nxt = exchange(
        buffer[:, :, lo:lo + halo, lo:hz].reshape(slab_y),
        buffer[:, :, hy - halo:hy, lo:hz].reshape(slab_y),
        "gy",
    )
    buffer = buffer.at[:, :, 0:lo, lo:hz].set(prev.reshape(nf, nx, halo, cells_z))
    buffer = buffer.at[:, :, hy:, lo:hz].set(nxt.reshape(nf, nx, halo, cells_z))

    def pack(a):
        return jnp.moveaxis(a, 3, 1).reshape(nf * halo, nx * ny)

    def unpack(a):
        return jnp.moveaxis(a.reshape(nf, halo, nx, ny), 1, 3)

    prev, nxt = exchange(
        pack(buffer[..., lo:lo + halo]), pack(buffer[..., hz - halo:hz]), "gz"
    )
    buffer = buffer.at[..., 0:lo].set(unpack(prev))
    buffer = buffer.at[..., hz:].set(unpack(nxt))
    eps_w, potential, forcing_w, coupling_w = buffer[0], buffer[1], buffer[2], buffer[3]

    coefficients = face_coefficients(eps_w)
    diagonal_sum = coefficients[0]
    for index in range(1, 6):
        diagonal_sum = diagonal_sum + coefficients[index]
    diagonal_sum = diagonal_sum + trim(coupling_w, 1)
    forcing_c = trim(forcing_w, 1)

    def inside_mask(k):
        def axis_mask(axis, cells):
            start = lax.axis_index(axis) * cells - k
            idx = start + jnp.arange(cells + 2 * k, dtype=jnp.int32)
            return (idx >= 0) & (idx < cells * lax.axis_size(axis))

        mx = axis_mask("gx", cells_x)
        my = axis_mask("gy", cells_y)
        mz = axis_mask("gz", cells_z)
        return mx[:, None, None] & my[None, :, None] & mz[None, None, :]

    for sweep in range(SWEEPS):
        k = halo - 1 - sweep
        off = sweep
        coeffs = [trim(c, off) for c in coefficients]
        neighbours = neighbour_sum(coeffs, potential)
        centre = potential[1:-1, 1:-1, 1:-1]
        updated = (1.0 - relaxation) * centre + relaxation * (
            trim(forcing_c, off) + neighbours
        ) / trim(diagonal_sum, off)
        if k > 0:
            updated = jnp.where(inside_mask(k), updated, 0.0)
        potential = updated

    off = SWEEPS
    coeffs = [trim(c, off) for c in coefficients]
    neighbours = neighbour_sum(coeffs, potential)
    centre = potential[1:-1, 1:-1, 1:-1]
    residual = trim(forcing_c, off) + neighbours - trim(diagonal_sum, off) * centre
    local_total = jnp.sum(residual * residual)
    device_count = grid_x * grid_y * grid_z
    gathered = lax.all_to_all(
        jnp.full((device_count,), local_total),
        ("gx", "gy", "gz"),
        split_axis=0,
        concat_axis=0,
        tiled=True,
    )
    squared_total = jnp.sum(gathered)
    cell_count = cells_x * cells_y * cells_z * device_count
    residual_norm = jnp.sqrt(squared_total / cell_count)
    return (centre, residual_norm)


def solution(mesh):
    in_specs = (
        P("gx", "gy", "gz"),
        P("gx", "gy", "gz"),
        P(),
        P("gz"),
        P(),
        P(("gx", "gy", "gz"), None),
        P(("gx", "gy", "gz")),
        P(("gx", "gy", "gz")),
        P(("gx", "gy", "gz")),
        P("gx", "gy", "gz"),
    )
    out_specs = (P("gx", "gy", "gz"), P())
    return jax.shard_map(
        on_device, mesh=mesh, in_specs=in_specs, out_specs=out_specs, check_vma=False
    )
```

```python
import jax
import jax.numpy as jnp
from jax import lax
from jax.sharding import PartitionSpec as P

SWEEPS = 4


relaxation = 0.8


def table_lookup(table, indices):
    labels = jnp.arange(table.shape[0], dtype=jnp.int32)
    matches = indices[:, None] == labels[None, :]
    return jnp.sum(jnp.where(matches, table[None, :], 0.0), axis=1)


def exchange(lo, hi, axis):
    count = lax.axis_size(axis)
    forward = [(i, i + 1) for i in range(count - 1)]
    backward = [(i + 1, i) for i in range(count - 1)]
    from_prev = lax.ppermute(hi, axis, forward)
    from_next = lax.ppermute(lo, axis, backward)
    return from_prev, from_next


def exchange_x(fields, width):
    return exchange(fields[:, :width], fields[:, -width:], "gx")


def with_wide_halo(fields, width):
    nf, nx, ny, nz = fields.shape

    def pack_y(a):
        return a.reshape(nf * nx * width, nz)

    def unpack_y(a):
        return a.reshape(nf, nx, width, nz)

    prev, nxt = exchange(pack_y(fields[:, :, :width]), pack_y(fields[:, :, -width:]), "gy")
    fields = jnp.concatenate([unpack_y(prev), fields, unpack_y(nxt)], axis=2)
    nf, nx, ny, _ = fields.shape

    def pack(a):
        return jnp.moveaxis(a, 3, 1).reshape(nf * width, nx * ny)

    def unpack(a):
        return jnp.moveaxis(a.reshape(nf, width, nx, ny), 1, 3)

    prev, nxt = exchange(pack(fields[..., :width]), pack(fields[..., -width:]), "gz")
    nz = fields.shape[3]
    wide = jnp.pad(fields, ((0, 0), (0, 0), (0, 0), (width, width)))
    wide = lax.dynamic_update_slice(wide, unpack(prev), (0, 0, 0, 0))
    return lax.dynamic_update_slice(wide, unpack(nxt), (0, 0, 0, nz + width))


def shifted(padded):
    return [
        padded[:-2, 1:-1, 1:-1],
        padded[2:, 1:-1, 1:-1],
        padded[1:-1, :-2, 1:-1],
        padded[1:-1, 2:, 1:-1],
        padded[1:-1, 1:-1, :-2],
        padded[1:-1, 1:-1, 2:],
    ]


def face_coefficients(padded):
    centre = padded[1:-1, 1:-1, 1:-1]
    result = []
    for neighbour in shifted(padded):
        result.append(2.0 * centre * neighbour / (centre + neighbour))
    return result


def neighbour_sum(coefficients, padded):
    pieces = shifted(padded)
    total_sum = coefficients[0] * pieces[0]
    for index in range(1, 6):
        total_sum = total_sum + coefficients[index] * pieces[index]
    return total_sum


def trim(a, k):
    if k == 0:
        return a
    return a[k:-k, k:-k, k:-k]


def on_device(
    charge,
    texture,
    material_eps,
    layer_material,
    gate_volts,
    block_cond,
    block_gate,
    block_dest,
    block_column,
    initial,
):
    cells_x, cells_y, cells_z = charge.shape
    grid_x = lax.axis_size("gx")
    grid_y = lax.axis_size("gy")
    grid_z = lax.axis_size("gz")
    peer_count = grid_x * grid_y
    block_count = block_dest.shape[0]
    capacity = max(2, 4 * block_count // peer_count)
    slot_total = peer_count * capacity
    layer_eps = table_lookup(material_eps, layer_material)
    permittivity = texture * layer_eps[None, None, :]

    same_dest = block_dest[:, None] == block_dest[None, :]
    order = jnp.arange(block_count, dtype=jnp.int32)
    earlier = order[None, :] < order[:, None]
    slot_rank = jnp.sum((same_dest & earlier).astype(jnp.int32), axis=1)
    position = block_dest * capacity + slot_rank
    block_volts = table_lookup(gate_volts, block_gate)
    rows = jnp.concatenate(
        [
            block_cond,
            block_volts[:, None],
            block_column.astype(jnp.float32)[:, None],
        ],
        axis=1,
    )
    width_row = cells_z + 2
    send = jnp.zeros((slot_total, width_row), jnp.float32).at[position].set(rows)
    send = send.reshape(peer_count, capacity * width_row)
    recv = lax.all_to_all(send, ("gx", "gy"), split_axis=0, concat_axis=0, tiled=True)
    recv = recv.reshape(slot_total, width_row)
    cond_recv = recv[:, :cells_z]
    volt_recv = recv[:, cells_z]
    column_recv = recv[:, cells_z + 1].astype(jnp.int32)
    extra_recv = cond_recv * volt_recv[:, None]
    columns = jnp.arange(cells_x * cells_y, dtype=jnp.int32)
    one_hot = (columns[:, None] == column_recv[None, :]).astype(jnp.float32)
    summed = jnp.dot(
        one_hot,
        jnp.concatenate([cond_recv, extra_recv], axis=1),
        precision=lax.Precision.HIGHEST,
        preferred_element_type=jnp.float32,
    )
    coupling = summed[:, :cells_z].reshape(cells_x, cells_y, cells_z)
    injected = summed[:, cells_z:].reshape(cells_x, cells_y, cells_z)
    forcing = charge + injected

    halo = SWEEPS + 1
    early = jnp.stack([permittivity, initial], axis=0)
    early_prev, early_next = exchange_x(early, halo)
    late = jnp.stack([forcing, coupling], axis=0)
    late_prev, late_next = exchange_x(late, halo - 1)
    pad = jnp.zeros((2, 1, cells_y, cells_z), jnp.float32)
    late_prev = jnp.concatenate([pad, late_prev], axis=1)
    late_next = jnp.concatenate([late_next, pad], axis=1)
    fields_x = jnp.concatenate(
        [
            jnp.concatenate([early_prev, early, early_next], axis=1),
            jnp.concatenate([late_prev, late, late_next], axis=1),
        ],
        axis=0,
    )
    wide = with_wide_halo(fields_x, halo)
    eps_w, initial_w, forcing_w, coupling_w = wide[0], wide[1], wide[2], wide[3]
    potential = initial_w

    coefficients = face_coefficients(eps_w)
    diagonal_sum = coefficients[0]
    for index in range(1, 6):
        diagonal_sum = diagonal_sum + coefficients[index]
    diagonal_sum = diagonal_sum + trim(coupling_w, 1)
    forcing_c = trim(forcing_w, 1)

    def inside_mask(k):
        def axis_mask(axis, cells):
            start = lax.axis_index(axis) * cells - k
            idx = start + jnp.arange(cells + 2 * k, dtype=jnp.int32)
            return (idx >= 0) & (idx < cells * lax.axis_size(axis))

        mx = axis_mask("gx", cells_x)
        my = axis_mask("gy", cells_y)
        mz = axis_mask("gz", cells_z)
        return mx[:, None, None] & my[None, :, None] & mz[None, None, :]

    for sweep in range(SWEEPS):
        k = halo - 1 - sweep
        off = sweep
        coeffs = [trim(c, off) for c in coefficients]
        neighbours = neighbour_sum(coeffs, potential)
        centre = potential[1:-1, 1:-1, 1:-1]
        updated = (1.0 - relaxation) * centre + relaxation * (
            trim(forcing_c, off) + neighbours
        ) / trim(diagonal_sum, off)
        if k > 0:
            updated = jnp.where(inside_mask(k), updated, 0.0)
        potential = updated

    off = SWEEPS
    coeffs = [trim(c, off) for c in coefficients]
    neighbours = neighbour_sum(coeffs, potential)
    centre = potential[1:-1, 1:-1, 1:-1]
    residual = trim(forcing_c, off) + neighbours - trim(diagonal_sum, off) * centre
    local_total = jnp.sum(residual * residual)
    device_count = grid_x * grid_y * grid_z
    gathered = lax.all_to_all(
        jnp.full((device_count,), local_total),
        ("gx", "gy", "gz"),
        split_axis=0,
        concat_axis=0,
        tiled=True,
    )
    squared_total = jnp.sum(gathered)
    cell_count = cells_x * cells_y * cells_z * device_count
    residual_norm = jnp.sqrt(squared_total / cell_count)
    return (centre, residual_norm)


def solution(mesh):
    in_specs = (
        P("gx", "gy", "gz"),
        P("gx", "gy", "gz"),
        P(),
        P("gz"),
        P(),
        P(("gx", "gy", "gz"), None),
        P(("gx", "gy", "gz")),
        P(("gx", "gy", "gz")),
        P(("gx", "gy", "gz")),
        P("gx", "gy", "gz"),
    )
    out_specs = (P("gx", "gy", "gz"), P())
    return jax.shard_map(
        on_device, mesh=mesh, in_specs=in_specs, out_specs=out_specs, check_vma=False
    )
```

```python
import jax
import jax.numpy as jnp
from jax import lax
from jax.sharding import PartitionSpec as P

SWEEPS = 4


relaxation = 0.8


def table_lookup(table, indices):
    labels = jnp.arange(table.shape[0], dtype=jnp.int32)
    matches = indices[:, None] == labels[None, :]
    return jnp.sum(jnp.where(matches, table[None, :], 0.0), axis=1)


def exchange(lo, hi, axis):
    count = lax.axis_size(axis)
    forward = [(i, i + 1) for i in range(count - 1)]
    backward = [(i + 1, i) for i in range(count - 1)]
    from_prev = lax.ppermute(hi, axis, forward)
    from_next = lax.ppermute(lo, axis, backward)
    return from_prev, from_next


def exchange_x(fields, width):
    return exchange(fields[:, :width], fields[:, -width:], "gx")


def with_wide_halo(fields, width):
    nf, nx, ny, nz = fields.shape

    def pack_y(a):
        return a.reshape(nf * nx * width, nz)

    def unpack_y(a):
        return a.reshape(nf, nx, width, nz)

    prev, nxt = exchange(pack_y(fields[:, :, :width]), pack_y(fields[:, :, -width:]), "gy")
    fields = jnp.concatenate([unpack_y(prev), fields, unpack_y(nxt)], axis=2)
    nf, nx, ny, _ = fields.shape

    def pack(a):
        return jnp.moveaxis(a, 3, 1).reshape(nf * width, nx * ny)

    def unpack(a):
        return jnp.moveaxis(a.reshape(nf, width, nx, ny), 1, 3)

    prev, nxt = exchange(pack(fields[..., :width]), pack(fields[..., -width:]), "gz")
    return jnp.concatenate([unpack(prev), fields, unpack(nxt)], axis=3)


def shifted(padded):
    return [
        padded[:-2, 1:-1, 1:-1],
        padded[2:, 1:-1, 1:-1],
        padded[1:-1, :-2, 1:-1],
        padded[1:-1, 2:, 1:-1],
        padded[1:-1, 1:-1, :-2],
        padded[1:-1, 1:-1, 2:],
    ]


def face_coefficients(padded):
    centre = padded[1:-1, 1:-1, 1:-1]
    result = []
    for neighbour in shifted(padded):
        result.append(2.0 * centre * neighbour / (centre + neighbour))
    return result


def neighbour_sum(coefficients, padded):
    pieces = shifted(padded)
    total_sum = coefficients[0] * pieces[0]
    for index in range(1, 6):
        total_sum = total_sum + coefficients[index] * pieces[index]
    return total_sum


def trim(a, k):
    if k == 0:
        return a
    return a[k:-k, k:-k, k:-k]


def on_device(
    charge,
    texture,
    material_eps,
    layer_material,
    gate_volts,
    block_cond,
    block_gate,
    block_dest,
    block_column,
    initial,
):
    cells_x, cells_y, cells_z = charge.shape
    grid_x = lax.axis_size("gx")
    grid_y = lax.axis_size("gy")
    grid_z = lax.axis_size("gz")
    peer_count = grid_x * grid_y
    block_count = block_dest.shape[0]
    capacity = max(2, 4 * block_count // peer_count)
    slot_total = peer_count * capacity
    layer_eps = table_lookup(material_eps, layer_material)
    permittivity = texture * layer_eps[None, None, :]

    same_dest = block_dest[:, None] == block_dest[None, :]
    order = jnp.arange(block_count, dtype=jnp.int32)
    earlier = order[None, :] < order[:, None]
    slot_rank = jnp.sum((same_dest & earlier).astype(jnp.int32), axis=1)
    position = block_dest * capacity + slot_rank
    block_volts = table_lookup(gate_volts, block_gate)
    rows = jnp.concatenate(
        [
            block_cond,
            block_volts[:, None],
            block_column.astype(jnp.float32)[:, None],
        ],
        axis=1,
    )
    width_row = cells_z + 2
    slots = jnp.arange(slot_total, dtype=jnp.int32)
    placement = (slots[:, None] == position[None, :]).astype(jnp.float32)
    send = jnp.dot(
        placement, rows, precision=lax.Precision.HIGHEST, preferred_element_type=jnp.float32
    )
    send = send.reshape(peer_count, capacity * width_row)
    recv = lax.all_to_all(send, ("gx", "gy"), split_axis=0, concat_axis=0, tiled=True)
    recv = recv.reshape(slot_total, width_row)
    cond_recv = recv[:, :cells_z]
    volt_recv = recv[:, cells_z]
    column_recv = recv[:, cells_z + 1].astype(jnp.int32)
    extra_recv = cond_recv * volt_recv[:, None]
    columns = jnp.arange(cells_x * cells_y, dtype=jnp.int32)
    one_hot = (columns[:, None] == column_recv[None, :]).astype(jnp.float32)
    summed = jnp.dot(
        one_hot,
        jnp.concatenate([cond_recv, extra_recv], axis=1),
        precision=lax.Precision.HIGHEST,
        preferred_element_type=jnp.float32,
    )
    coupling = summed[:, :cells_z].reshape(cells_x, cells_y, cells_z)
    injected = summed[:, cells_z:].reshape(cells_x, cells_y, cells_z)
    forcing = charge + injected

    halo = SWEEPS + 1
    early = jnp.stack([permittivity, initial], axis=0)
    early_prev, early_next = exchange_x(early, halo)
    late = jnp.stack([forcing, coupling], axis=0)
    late_prev, late_next = exchange_x(late, halo - 1)
    pad = jnp.zeros((2, 1, cells_y, cells_z), jnp.float32)
    late_prev = jnp.concatenate([pad, late_prev], axis=1)
    late_next = jnp.concatenate([late_next, pad], axis=1)
    fields_x = jnp.concatenate(
        [
            jnp.concatenate([early_prev, early, early_next], axis=1),
            jnp.concatenate([late_prev, late, late_next], axis=1),
        ],
        axis=0,
    )
    wide = with_wide_halo(fields_x, halo)
    eps_w, initial_w, forcing_w, coupling_w = wide[0], wide[1], wide[2], wide[3]
    potential = initial_w

    coefficients = face_coefficients(eps_w)
    diagonal_sum = coefficients[0]
    for index in range(1, 6):
        diagonal_sum = diagonal_sum + coefficients[index]
    diagonal_sum = diagonal_sum + trim(coupling_w, 1)
    forcing_c = trim(forcing_w, 1)

    def inside_mask(k):
        def axis_mask(axis, cells):
            start = lax.axis_index(axis) * cells - k
            idx = start + jnp.arange(cells + 2 * k, dtype=jnp.int32)
            return (idx >= 0) & (idx < cells * lax.axis_size(axis))

        mx = axis_mask("gx", cells_x)
        my = axis_mask("gy", cells_y)
        mz = axis_mask("gz", cells_z)
        return mx[:, None, None] & my[None, :, None] & mz[None, None, :]

    for sweep in range(SWEEPS):
        k = halo - 1 - sweep
        off = sweep
        coeffs = [trim(c, off) for c in coefficients]
        neighbours = neighbour_sum(coeffs, potential)
        centre = potential[1:-1, 1:-1, 1:-1]
        updated = (1.0 - relaxation) * centre + relaxation * (
            trim(forcing_c, off) + neighbours
        ) / trim(diagonal_sum, off)
        if k > 0:
            updated = jnp.where(inside_mask(k), updated, 0.0)
        potential = updated

    off = SWEEPS
    coeffs = [trim(c, off) for c in coefficients]
    neighbours = neighbour_sum(coeffs, potential)
    centre = potential[1:-1, 1:-1, 1:-1]
    residual = trim(forcing_c, off) + neighbours - trim(diagonal_sum, off) * centre
    local_total = jnp.sum(residual * residual)
    device_count = grid_x * grid_y * grid_z
    gathered = lax.all_to_all(
        jnp.full((device_count,), local_total),
        ("gx", "gy", "gz"),
        split_axis=0,
        concat_axis=0,
        tiled=True,
    )
    squared_total = jnp.sum(gathered)
    cell_count = cells_x * cells_y * cells_z * device_count
    residual_norm = jnp.sqrt(squared_total / cell_count)
    return (centre, residual_norm)


def solution(mesh):
    in_specs = (
        P("gx", "gy", "gz"),
        P("gx", "gy", "gz"),
        P(),
        P("gz"),
        P(),
        P(("gx", "gy", "gz"), None),
        P(("gx", "gy", "gz")),
        P(("gx", "gy", "gz")),
        P(("gx", "gy", "gz")),
        P("gx", "gy", "gz"),
    )
    out_specs = (P("gx", "gy", "gz"), P())
    return jax.shard_map(
        on_device, mesh=mesh, in_specs=in_specs, out_specs=out_specs, check_vma=False
    )
```

```python
import jax
import jax.numpy as jnp
from jax import lax
from jax.sharding import PartitionSpec as P

SWEEPS = 4


relaxation = 0.8


def table_lookup(table, indices):
    labels = jnp.arange(table.shape[0], dtype=jnp.int32)
    matches = indices[:, None] == labels[None, :]
    return jnp.sum(jnp.where(matches, table[None, :], 0.0), axis=1)


def exchange(lo, hi, axis):
    count = lax.axis_size(axis)
    forward = [(i, i + 1) for i in range(count - 1)]
    backward = [(i + 1, i) for i in range(count - 1)]
    from_prev = lax.ppermute(hi, axis, forward)
    from_next = lax.ppermute(lo, axis, backward)
    return from_prev, from_next


def exchange_x(fields, width):
    return exchange(fields[:, :width], fields[:, -width:], "gx")


def with_wide_halo(fields, width):
    nf, nx, ny, nz = fields.shape

    def pack_y(a):
        return a.reshape(nf * nx * width, nz)

    def unpack_y(a):
        return a.reshape(nf, nx, width, nz)

    prev, nxt = exchange(pack_y(fields[:, :, :width]), pack_y(fields[:, :, -width:]), "gy")
    fields = jnp.concatenate([unpack_y(prev), fields, unpack_y(nxt)], axis=2)
    nf, nx, ny, _ = fields.shape

    def pack(a):
        return jnp.moveaxis(a, 3, 1).reshape(nf * width, nx * ny)

    def unpack(a):
        return jnp.moveaxis(a.reshape(nf, width, nx, ny), 1, 3)

    prev, nxt = exchange(pack(fields[..., :width]), pack(fields[..., -width:]), "gz")
    return jnp.concatenate([unpack(prev), fields, unpack(nxt)], axis=3)


def shifted(padded):
    return [
        padded[:-2, 1:-1, 1:-1],
        padded[2:, 1:-1, 1:-1],
        padded[1:-1, :-2, 1:-1],
        padded[1:-1, 2:, 1:-1],
        padded[1:-1, 1:-1, :-2],
        padded[1:-1, 1:-1, 2:],
    ]


def face_coefficients(padded):
    centre = padded[1:-1, 1:-1, 1:-1]
    result = []
    for neighbour in shifted(padded):
        result.append(2.0 * centre * neighbour / (centre + neighbour))
    return result


def neighbour_sum(coefficients, padded):
    pieces = shifted(padded)
    total_sum = coefficients[0] * pieces[0]
    for index in range(1, 6):
        total_sum = total_sum + coefficients[index] * pieces[index]
    return total_sum


def trim(a, k):
    if k == 0:
        return a
    return a[k:-k, k:-k, k:-k]


def on_device(
    charge,
    texture,
    material_eps,
    layer_material,
    gate_volts,
    block_cond,
    block_gate,
    block_dest,
    block_column,
    initial,
):
    cells_x, cells_y, cells_z = charge.shape
    grid_x = lax.axis_size("gx")
    grid_y = lax.axis_size("gy")
    grid_z = lax.axis_size("gz")
    peer_count = grid_x * grid_y
    block_count = block_dest.shape[0]
    capacity = max(2, 4 * block_count // peer_count)
    slot_total = peer_count * capacity
    layer_eps = table_lookup(material_eps, layer_material)
    permittivity = texture * layer_eps[None, None, :]

    same_dest = block_dest[:, None] == block_dest[None, :]
    order = jnp.arange(block_count, dtype=jnp.int32)
    earlier = order[None, :] < order[:, None]
    slot_rank = jnp.sum((same_dest & earlier).astype(jnp.int32), axis=1)
    block_volts = table_lookup(gate_volts, block_gate)
    meta = jnp.stack([block_volts, block_column.astype(jnp.float32)], axis=1)
    peers = jnp.arange(peer_count, dtype=jnp.int32)
    to_peer = peers[:, None] == block_dest[None, :]
    cond_parts, meta_parts = [], []
    for slot in range(capacity):
        pick = (to_peer & (slot_rank[None, :] == slot)).astype(jnp.float32)
        cond_parts.append(
            jnp.dot(pick, block_cond, precision=lax.Precision.HIGHEST, preferred_element_type=jnp.float32)
        )
        meta_parts.append(
            jnp.dot(pick, meta, precision=lax.Precision.HIGHEST, preferred_element_type=jnp.float32)
        )
    send = jnp.concatenate(cond_parts + meta_parts, axis=1)
    recv = lax.all_to_all(send, ("gx", "gy"), split_axis=0, concat_axis=0, tiled=True)
    cond_recv = jnp.concatenate(
        [recv[:, slot * cells_z:(slot + 1) * cells_z] for slot in range(capacity)], axis=0
    )
    meta_base = capacity * cells_z
    volt_recv = jnp.concatenate(
        [recv[:, meta_base + 2 * slot] for slot in range(capacity)], axis=0
    )
    column_recv = jnp.concatenate(
        [recv[:, meta_base + 2 * slot + 1] for slot in range(capacity)], axis=0
    ).astype(jnp.int32)
    extra_recv = cond_recv * volt_recv[:, None]
    columns = jnp.arange(cells_x * cells_y, dtype=jnp.int32)
    one_hot = (columns[:, None] == column_recv[None, :]).astype(jnp.float32)
    summed = jnp.dot(
        one_hot,
        jnp.concatenate([cond_recv, extra_recv], axis=1),
        precision=lax.Precision.HIGHEST,
        preferred_element_type=jnp.float32,
    )
    coupling = summed[:, :cells_z].reshape(cells_x, cells_y, cells_z)
    injected = summed[:, cells_z:].reshape(cells_x, cells_y, cells_z)
    forcing = charge + injected

    halo = SWEEPS + 1
    early = jnp.stack([permittivity, initial], axis=0)
    early_prev, early_next = exchange_x(early, halo)
    late = jnp.stack([forcing, coupling], axis=0)
    late_prev, late_next = exchange_x(late, halo - 1)
    pad = jnp.zeros((2, 1, cells_y, cells_z), jnp.float32)
    late_prev = jnp.concatenate([pad, late_prev], axis=1)
    late_next = jnp.concatenate([late_next, pad], axis=1)
    fields_x = jnp.concatenate(
        [
            jnp.concatenate([early_prev, early, early_next], axis=1),
            jnp.concatenate([late_prev, late, late_next], axis=1),
        ],
        axis=0,
    )
    wide = with_wide_halo(fields_x, halo)
    eps_w, initial_w, forcing_w, coupling_w = wide[0], wide[1], wide[2], wide[3]
    potential = initial_w

    coefficients = face_coefficients(eps_w)
    diagonal_sum = coefficients[0]
    for index in range(1, 6):
        diagonal_sum = diagonal_sum + coefficients[index]
    diagonal_sum = diagonal_sum + trim(coupling_w, 1)
    forcing_c = trim(forcing_w, 1)

    def inside_mask(k):
        def axis_mask(axis, cells):
            start = lax.axis_index(axis) * cells - k
            idx = start + jnp.arange(cells + 2 * k, dtype=jnp.int32)
            return (idx >= 0) & (idx < cells * lax.axis_size(axis))

        mx = axis_mask("gx", cells_x)
        my = axis_mask("gy", cells_y)
        mz = axis_mask("gz", cells_z)
        return mx[:, None, None] & my[None, :, None] & mz[None, None, :]

    for sweep in range(SWEEPS):
        k = halo - 1 - sweep
        off = sweep
        coeffs = [trim(c, off) for c in coefficients]
        neighbours = neighbour_sum(coeffs, potential)
        centre = potential[1:-1, 1:-1, 1:-1]
        updated = (1.0 - relaxation) * centre + relaxation * (
            trim(forcing_c, off) + neighbours
        ) / trim(diagonal_sum, off)
        if k > 0:
            updated = jnp.where(inside_mask(k), updated, 0.0)
        potential = updated

    off = SWEEPS
    coeffs = [trim(c, off) for c in coefficients]
    neighbours = neighbour_sum(coeffs, potential)
    centre = potential[1:-1, 1:-1, 1:-1]
    residual = trim(forcing_c, off) + neighbours - trim(diagonal_sum, off) * centre
    local_total = jnp.sum(residual * residual)
    device_count = grid_x * grid_y * grid_z
    gathered = lax.all_to_all(
        jnp.full((device_count,), local_total),
        ("gx", "gy", "gz"),
        split_axis=0,
        concat_axis=0,
        tiled=True,
    )
    squared_total = jnp.sum(gathered)
    cell_count = cells_x * cells_y * cells_z * device_count
    residual_norm = jnp.sqrt(squared_total / cell_count)
    return (centre, residual_norm)


def solution(mesh):
    in_specs = (
        P("gx", "gy", "gz"),
        P("gx", "gy", "gz"),
        P(),
        P("gz"),
        P(),
        P(("gx", "gy", "gz"), None),
        P(("gx", "gy", "gz")),
        P(("gx", "gy", "gz")),
        P(("gx", "gy", "gz")),
        P("gx", "gy", "gz"),
    )
    out_specs = (P("gx", "gy", "gz"), P())
    return jax.shard_map(
        on_device, mesh=mesh, in_specs=in_specs, out_specs=out_specs, check_vma=False
    )
```

```python
import jax
import jax.numpy as jnp
from jax import lax
from jax.sharding import PartitionSpec as P

SWEEPS = 4


relaxation = 0.8


def table_lookup(table, indices):
    labels = jnp.arange(table.shape[0], dtype=jnp.int32)
    matches = indices[:, None] == labels[None, :]
    return jnp.sum(jnp.where(matches, table[None, :], 0.0), axis=1)


def exchange(lo, hi, axis):
    count = lax.axis_size(axis)
    forward = [(i, i + 1) for i in range(count - 1)]
    backward = [(i + 1, i) for i in range(count - 1)]
    from_prev = lax.ppermute(hi, axis, forward)
    from_next = lax.ppermute(lo, axis, backward)
    return from_prev, from_next


def exchange_x(fields, width):
    return exchange(fields[:, :width], fields[:, -width:], "gx")


def with_wide_halo(fields, width):
    nf, nx, ny, nz = fields.shape

    def pack_y(a):
        return a.reshape(nf * nx * width, nz)

    def unpack_y(a):
        return a.reshape(nf, nx, width, nz)

    prev, nxt = exchange(pack_y(fields[:, :, :width]), pack_y(fields[:, :, -width:]), "gy")
    fields = jnp.concatenate([unpack_y(prev), fields, unpack_y(nxt)], axis=2)
    nf, nx, ny, _ = fields.shape

    def pack(a):
        return jnp.moveaxis(a, 3, 1).reshape(nf * width, nx * ny)

    def unpack(a):
        return jnp.moveaxis(a.reshape(nf, width, nx, ny), 1, 3)

    prev, nxt = exchange(pack(fields[..., :width]), pack(fields[..., -width:]), "gz")
    return jnp.concatenate([unpack(prev), fields, unpack(nxt)], axis=3)


def shifted(padded):
    return [
        padded[:-2, 1:-1, 1:-1],
        padded[2:, 1:-1, 1:-1],
        padded[1:-1, :-2, 1:-1],
        padded[1:-1, 2:, 1:-1],
        padded[1:-1, 1:-1, :-2],
        padded[1:-1, 1:-1, 2:],
    ]


def face_coefficients(padded):
    centre = padded[1:-1, 1:-1, 1:-1]
    result = []
    for neighbour in shifted(padded):
        result.append(2.0 * centre * neighbour / (centre + neighbour))
    return result


def neighbour_sum(coefficients, padded):
    pieces = shifted(padded)
    total_sum = coefficients[0] * pieces[0]
    for index in range(1, 6):
        total_sum = total_sum + coefficients[index] * pieces[index]
    return total_sum


def trim(a, k):
    if k == 0:
        return a
    return a[k:-k, k:-k, k:-k]


def on_device(
    charge,
    texture,
    material_eps,
    layer_material,
    gate_volts,
    block_cond,
    block_gate,
    block_dest,
    block_column,
    initial,
):
    cells_x, cells_y, cells_z = charge.shape
    grid_x = lax.axis_size("gx")
    grid_y = lax.axis_size("gy")
    grid_z = lax.axis_size("gz")
    peer_count = grid_x * grid_y
    block_count = block_dest.shape[0]
    capacity = max(2, 4 * block_count // peer_count)
    slot_total = peer_count * capacity
    layer_eps = table_lookup(material_eps, layer_material)
    permittivity = texture * layer_eps[None, None, :]

    same_dest = block_dest[:, None] == block_dest[None, :]
    order = jnp.arange(block_count, dtype=jnp.int32)
    earlier = order[None, :] < order[:, None]
    slot_rank = jnp.sum((same_dest & earlier).astype(jnp.int32), axis=1)
    position = block_dest * capacity + slot_rank
    gate_labels = jnp.arange(gate_volts.shape[0], dtype=jnp.int32)
    gate_pick = (block_gate[:, None] == gate_labels[None, :]).astype(jnp.float32)
    block_volts = jnp.dot(
        gate_pick, gate_volts, precision=lax.Precision.HIGHEST, preferred_element_type=jnp.float32
    )
    rows = jnp.concatenate(
        [
            block_cond,
            block_volts[:, None],
            block_column.astype(jnp.float32)[:, None],
        ],
        axis=1,
    )
    width_row = cells_z + 2
    slots = jnp.arange(slot_total, dtype=jnp.int32)
    placement = (slots[:, None] == position[None, :]).astype(jnp.float32)
    send = jnp.dot(
        placement, rows, precision=lax.Precision.HIGHEST, preferred_element_type=jnp.float32
    )
    send = send.reshape(peer_count, capacity * width_row)
    recv = lax.all_to_all(send, ("gx", "gy"), split_axis=0, concat_axis=0, tiled=True)
    recv = recv.reshape(slot_total, width_row)
    cond_recv = recv[:, :cells_z]
    volt_recv = recv[:, cells_z]
    column_recv = recv[:, cells_z + 1].astype(jnp.int32)
    extra_recv = cond_recv * volt_recv[:, None]
    columns = jnp.arange(cells_x * cells_y, dtype=jnp.int32)
    one_hot = (columns[:, None] == column_recv[None, :]).astype(jnp.float32)
    summed = jnp.dot(
        one_hot,
        jnp.concatenate([cond_recv, extra_recv], axis=1),
        precision=lax.Precision.HIGHEST,
        preferred_element_type=jnp.float32,
    )
    coupling = summed[:, :cells_z].reshape(cells_x, cells_y, cells_z)
    injected = summed[:, cells_z:].reshape(cells_x, cells_y, cells_z)
    forcing = charge + injected

    halo = SWEEPS + 1
    early = jnp.stack([permittivity, initial], axis=0)
    early_prev, early_next = exchange_x(early, halo)
    late = jnp.stack([forcing, coupling], axis=0)
    late_prev, late_next = exchange_x(late, halo - 1)
    pad = jnp.zeros((2, 1, cells_y, cells_z), jnp.float32)
    late_prev = jnp.concatenate([pad, late_prev], axis=1)
    late_next = jnp.concatenate([late_next, pad], axis=1)
    fields_x = jnp.concatenate(
        [
            jnp.concatenate([early_prev, early, early_next], axis=1),
            jnp.concatenate([late_prev, late, late_next], axis=1),
        ],
        axis=0,
    )
    wide = with_wide_halo(fields_x, halo)
    eps_w, initial_w, forcing_w, coupling_w = wide[0], wide[1], wide[2], wide[3]
    potential = initial_w

    coefficients = face_coefficients(eps_w)
    diagonal_sum = coefficients[0]
    for index in range(1, 6):
        diagonal_sum = diagonal_sum + coefficients[index]
    diagonal_sum = diagonal_sum + trim(coupling_w, 1)
    forcing_c = trim(forcing_w, 1)

    def inside_mask(k):
        def axis_mask(axis, cells):
            start = lax.axis_index(axis) * cells - k
            idx = start + jnp.arange(cells + 2 * k, dtype=jnp.int32)
            return (idx >= 0) & (idx < cells * lax.axis_size(axis))

        mx = axis_mask("gx", cells_x)
        my = axis_mask("gy", cells_y)
        mz = axis_mask("gz", cells_z)
        return mx[:, None, None] & my[None, :, None] & mz[None, None, :]

    for sweep in range(SWEEPS):
        k = halo - 1 - sweep
        off = sweep
        coeffs = [trim(c, off) for c in coefficients]
        neighbours = neighbour_sum(coeffs, potential)
        centre = potential[1:-1, 1:-1, 1:-1]
        updated = (1.0 - relaxation) * centre + relaxation * (
            trim(forcing_c, off) + neighbours
        ) / trim(diagonal_sum, off)
        if k > 0:
            updated = jnp.where(inside_mask(k), updated, 0.0)
        potential = updated

    off = SWEEPS
    coeffs = [trim(c, off) for c in coefficients]
    neighbours = neighbour_sum(coeffs, potential)
    centre = potential[1:-1, 1:-1, 1:-1]
    residual = trim(forcing_c, off) + neighbours - trim(diagonal_sum, off) * centre
    local_total = jnp.sum(residual * residual)
    device_count = grid_x * grid_y * grid_z
    gathered = lax.all_to_all(
        jnp.full((device_count,), local_total),
        ("gx", "gy", "gz"),
        split_axis=0,
        concat_axis=0,
        tiled=True,
    )
    squared_total = jnp.sum(gathered)
    cell_count = cells_x * cells_y * cells_z * device_count
    residual_norm = jnp.sqrt(squared_total / cell_count)
    return (centre, residual_norm)


def solution(mesh):
    in_specs = (
        P("gx", "gy", "gz"),
        P("gx", "gy", "gz"),
        P(),
        P("gz"),
        P(),
        P(("gx", "gy", "gz"), None),
        P(("gx", "gy", "gz")),
        P(("gx", "gy", "gz")),
        P(("gx", "gy", "gz")),
        P("gx", "gy", "gz"),
    )
    out_specs = (P("gx", "gy", "gz"), P())
    return jax.shard_map(
        on_device, mesh=mesh, in_specs=in_specs, out_specs=out_specs, check_vma=False
    )
```
